256 devices in a mesh: query: 8 (over x, core), bank: 32 (over z, y).
Axes of the slice: x: 4, y: 4, z: 8, core: 2. Of those that a mesh axis runs over, the one named last changes fastest.
Arguments:
- queries: bfloat16 [2048, 32, 128], P(('query', 'bank'))
- passages: bfloat16 [8192, 128, 128], P('bank')
- passage_home: int32 [8192], replicated, may hold values from 0 to 8191, as said below
- candidates: int32 [2048, 16], P(('query', 'bank')), may hold values from 0 to 8191, as said below
- positive: int32 [2048], P(('query', 'bank')), may hold values from 0 to 15
Outputs:
- losses: float32 [2048], P(('query', 'bank'))
- query_grads: float32 [2048, 32, 128], P(('query', 'bank'))
The draws below stay inside these ranges and needn't reach their ends.
Inputs may be any that keep to these rules, and one draw needn't show every extreme that they name: `passage_home`: each passage id has its own storage row; storage row r lies on bank index r // 256. `candidates`: among the 128 list entries of one device's queries (aligned blocks of 8 queries, in order), at most 12 name passages stored on one bank index; in every block some bank index gets exactly 12, and in each group of 32 consecutive blocks it is the same bank index for all of them.
All inputs are finite; a program needn't handle non-finite values.
Results may differ from the reference program's by a relative error of at most 0.0049.
Values may be sent and summed in bfloat16 or wider, within the bound.
No kernel may reach another device: no remote copies, remote signals or barrier semaphores. Data moves between devices by JAX's collectives and lax.ppermute only.
A program may use at most 128 MiB of HBM per device.

```python
import math
import jax
import jax.numpy as jnp
from jax import lax

DIM = 128
LQ = 32
LP = 128
K = 16
QD = 8
P_DEV = 256
NQ = 2048
NP = 8192
CAP = 12


def pair_plan(key):
    shard_count = NP // P_DEV
    passage_home = jax.random.permutation(jax.random.fold_in(key, 101), NP).astype(jnp.int32)
    blocks = NQ // QD
    entries = QD * K
    groups = blocks // shard_count
    hottest = jax.random.randint(jax.random.fold_in(key, 102), (groups,), 0, shard_count)
    hot_block = jnp.repeat(hottest, shard_count)
    shifting = jax.random.randint(jax.random.fold_in(key, 103), (blocks, 1), 0, shard_count - 1)
    counter = jnp.arange(entries, dtype=jnp.int32)[None, :]
    spread = (hot_block[:, None] + 1 + (counter - CAP + shifting) % (shard_count - 1)) % shard_count
    owners = jnp.where(counter < CAP, hot_block[:, None], spread).astype(jnp.int32)
    shuffle_keys = jax.random.split(jax.random.fold_in(key, 104), blocks)
    owners = jax.vmap(lambda k, v: jax.random.permutation(k, v))(shuffle_keys, owners)
    local_slots = jax.random.randint(jax.random.fold_in(key, 105), (blocks, entries), 0, P_DEV)
    storage = owners * P_DEV + local_slots
    inverse = jnp.argsort(passage_home).astype(jnp.int32)
    return (passage_home, inverse[storage].reshape(NQ, K).astype(jnp.int32))


def passage_rows(key, storage):
    base_key = jax.random.fold_in(key, 201)

    def one_row(row):
        row_key = jax.random.fold_in(base_key, row)
        return jax.random.truncated_normal(row_key, -4.0, 4.0, (LP, DIM), jnp.float32)
    return jax.vmap(one_row)(storage)


def draw_passage_home(key, part):
    return pair_plan(key)[0]


def draw_candidates(key, part):
    return pair_plan(key)[1]


def draw_passages(key, part):
    return passage_rows(key, jnp.arange(NP, dtype=jnp.int32)).astype(jnp.bfloat16)


def draw_queries(key, part):
    return (0.18 * jax.random.truncated_normal(jax.random.fold_in(key, 301), -4.0, 4.0, (NQ, LQ, DIM), jnp.float32)).astype(jnp.bfloat16)


def touch_ends(array, stream_key, low, high):
    extent = array.shape
    place = [jax.random.randint(jax.random.fold_in(stream_key, axis), (), 0, extent[axis]) for axis in range(len(extent))]
    array = array.at[tuple(place)].set(low)
    longest = extent.index(max(extent))
    place[longest] = (place[longest] + 1) % extent[longest]
    return array.at[tuple(place)].set(high)


def setup_inputs(seed: int = 0) -> dict:
    key_of = jax.random.split(jax.random.key(seed), 6)
    return {
        "queries": draw_queries(jax.random.fold_in(key_of[5], 71), 0),
        "passages": draw_passages(jax.random.fold_in(key_of[5], 71), 0),
        "passage_home": draw_passage_home(jax.random.fold_in(key_of[5], 71), 0),
        "candidates": draw_candidates(jax.random.fold_in(key_of[5], 71), 0),
        "positive": touch_ends(jax.random.randint(key_of[4], (NQ,), 0, K), jax.random.fold_in(key_of[4], 1), 0, K - 1).astype(jnp.int32),
    }


def pair_terms(query_tok, passage_tiles):
    scores = jnp.einsum("nid,njd->nij", query_tok.astype(jnp.float32), passage_tiles.astype(jnp.float32))
    largest = jnp.max(scores, axis=2, keepdims=True)
    raised = jnp.exp(scores - largest)
    totals = jnp.sum(raised, axis=2, keepdims=True)
    maxima = largest[:, :, 0] + jnp.log(totals[:, :, 0])
    weights = (raised / totals).astype(jnp.bfloat16)
    token_basis = jnp.einsum("nij,njd->nid", weights.astype(jnp.float32), passage_tiles.astype(jnp.float32)).astype(jnp.bfloat16)
    return maxima, token_basis


def contrast(maxima, positive):
    similarity = jnp.sum(maxima, axis=2)
    largest = jnp.max(similarity, axis=1, keepdims=True)
    raised = jnp.exp(similarity - largest)
    totals = jnp.sum(raised, axis=1, keepdims=True)
    picked = jnp.arange(similarity.shape[1], dtype=jnp.int32)[None, :] == positive[:, None]
    losses = largest[:, 0] + jnp.log(totals[:, 0]) - jnp.sum(jnp.where(picked, similarity, jnp.zeros_like(similarity)), axis=1)
    coefficients = (raised / totals - picked.astype(similarity.dtype)).astype(jnp.bfloat16)
    return losses, coefficients


def reference(queries, passages, passage_home, candidates, positive):
    block_rows = math.gcd(NQ, 32)
    storage = passage_home[candidates]

    def one_block(block_index):
        first_row = (block_index * block_rows).astype(jnp.int32)
        query_part = lax.dynamic_slice_in_dim(queries, first_row, block_rows, 0)
        storage_part = lax.dynamic_slice_in_dim(storage, first_row, block_rows, 0)
        positive_part = lax.dynamic_slice_in_dim(positive, first_row, block_rows, 0)
        passage_tiles = passages[storage_part.reshape(-1)]
        paired = jnp.repeat(query_part, K, axis=0)
        maxima, token_basis = pair_terms(paired, passage_tiles)
        losses, coefficients = contrast(maxima.reshape(block_rows, K, LQ), positive_part)
        gradient = jnp.einsum("qk,qkd->qd", coefficients.astype(jnp.float32), token_basis.reshape(block_rows, K, LQ * DIM).astype(jnp.float32))
        return losses, gradient.reshape(block_rows, LQ, DIM)

    losses, gradient = lax.map(one_block, jnp.arange(NQ // block_rows, dtype=jnp.int32))
    return losses.reshape(NQ), gradient.reshape(NQ, LQ, DIM)
```

```python
import jax
import jax.numpy as jnp
from jax import lax
from jax.sharding import PartitionSpec as P


def soft_terms(scores):
    largest = jnp.max(scores, axis=-1, keepdims=True)
    raised = jnp.exp(scores - largest)
    totals = jnp.sum(raised, axis=-1, keepdims=True)
    maxima = largest[..., 0] + jnp.log(totals[..., 0])
    weights = (raised / totals).astype(jnp.bfloat16)
    return (maxima, weights)


def contrast(similarity, positive):
    largest = jnp.max(similarity, axis=1, keepdims=True)
    raised = jnp.exp(similarity - largest)
    totals = jnp.sum(raised, axis=1, keepdims=True)
    picked = jnp.arange(similarity.shape[1], dtype=jnp.int32)[None, :] == positive[:, None]
    losses = (
        largest[:, 0] + jnp.log(totals[:, 0]) - jnp.sum(jnp.where(picked, similarity, 0.0), axis=1)
    )
    coefficients = (raised / totals - picked.astype(jnp.float32)).astype(jnp.bfloat16)
    return (losses, coefficients)


def body(queries, passages, passage_home, candidates, positive):
    shards = lax.axis_size("bank")
    me = lax.axis_index("bank")
    query_rows, query_len, feature_dim = queries.shape
    listed = candidates.shape[1]
    holdings = passages.shape[0]
    tile_len = passages.shape[1]
    entries = query_rows * listed
    capacity = 3 * entries // shards
    group_rows = shards * query_rows

    lists = jnp.concatenate([candidates, positive[:, None]], axis=1)
    lists = lax.all_gather(lists, "bank", axis=0, tiled=True)
    group_candidates = lists[:, :listed]
    group_positive = lists[:, listed]
    group_queries = lax.all_gather(queries, "bank", axis=0, tiled=True)

    storage = passage_home[group_candidates].reshape(shards, entries)
    mine = (storage // holdings) == me
    position = jnp.cumsum(mine.astype(jnp.int32), axis=1) - 1
    slot_ids = jnp.arange(capacity, dtype=jnp.int32)
    hit = mine[:, None, :] & (position[:, None, :] == slot_ids[None, :, None])
    valid = jnp.any(hit, axis=2)
    entry_ids = jnp.arange(entries, dtype=jnp.int32)
    entry = jnp.sum(jnp.where(hit, entry_ids[None, None, :], 0), axis=2)
    local_slot = jnp.sum(jnp.where(hit, (storage % holdings)[:, None, :], 0), axis=2)
    source = jnp.arange(shards, dtype=jnp.int32)[:, None]
    query_index = (source * query_rows + entry // listed).reshape(-1)
    flat_index = (source * entries + entry).reshape(-1)
    valid = valid.reshape(-1)
    local_slot = local_slot.reshape(-1)

    passage_tiles = passages[local_slot]
    query_tiles = group_queries[query_index]
    scores = jnp.einsum(
        "sid,sjd->sij", query_tiles, passage_tiles, preferred_element_type=jnp.float32
    )
    maxima, weights = soft_terms(scores)
    token_basis = jnp.einsum(
        "sij,sjd->sid", weights, passage_tiles, preferred_element_type=jnp.float32
    ).astype(jnp.bfloat16)

    slot_similarity = jnp.sum(maxima, axis=1)
    place = flat_index[:, None] == jnp.arange(group_rows * listed, dtype=jnp.int32)[None, :]
    place = place & valid[:, None]
    similarity = jnp.sum(jnp.where(place, slot_similarity[:, None], 0.0), axis=0)
    similarity = lax.psum(similarity, "bank").reshape(group_rows, listed)

    losses, coefficients = contrast(similarity, group_positive)
    slot_coefficient = jnp.where(
        valid, coefficients.reshape(-1)[flat_index], jnp.zeros((), jnp.bfloat16)
    )
    owner = query_index[:, None] == jnp.arange(group_rows, dtype=jnp.int32)[None, :]
    spread = jnp.where(owner, slot_coefficient[:, None], jnp.zeros((), jnp.bfloat16))
    partial = jnp.einsum(
        "sq,sd->qd",
        spread,
        token_basis.reshape(-1, query_len * feature_dim),
        preferred_element_type=jnp.float32,
    )
    gradient = lax.psum_scatter(partial, "bank", scatter_dimension=0, tiled=True)
    own_losses = lax.dynamic_slice_in_dim(losses, me * query_rows, query_rows)
    return (own_losses, gradient.reshape(query_rows, query_len, feature_dim))


def solution(mesh):
    return jax.shard_map(
        body,
        mesh=mesh,
        in_specs=(
            P(("query", "bank"), None, None),
            P("bank", None, None),
            P(),
            P(("query", "bank"), None),
            P(("query", "bank")),
        ),
        out_specs=(P(("query", "bank")), P(("query", "bank"), None, None)),
        check_vma=False,
    )
```

```python
import jax
import jax.numpy as jnp
import numpy as np
from jax import lax
from jax.sharding import Mesh
from jax.sharding import PartitionSpec as P

BANK = ("z", "y")


def soft_terms(scores):
    largest = jnp.max(scores, axis=-1, keepdims=True)
    raised = jnp.exp(scores - largest)
    totals = jnp.sum(raised, axis=-1, keepdims=True)
    maxima = largest[..., 0] + jnp.log(totals[..., 0])
    weights = (raised / totals).astype(jnp.bfloat16)
    return (maxima, weights)


def contrast(similarity, positive):
    largest = jnp.max(similarity, axis=1, keepdims=True)
    raised = jnp.exp(similarity - largest)
    totals = jnp.sum(raised, axis=1, keepdims=True)
    picked = jnp.arange(similarity.shape[1], dtype=jnp.int32)[None, :] == positive[:, None]
    losses = (
        largest[:, 0] + jnp.log(totals[:, 0]) - jnp.sum(jnp.where(picked, similarity, 0.0), axis=1)
    )
    coefficients = (raised / totals - picked.astype(jnp.float32)).astype(jnp.bfloat16)
    return (losses, coefficients)


def split3(value):
    high = lax.reduce_precision(value, exponent_bits=8, mantissa_bits=7)
    rest = value - high
    middle = lax.reduce_precision(rest, exponent_bits=8, mantissa_bits=7)
    low = rest - middle
    return jnp.stack([high, middle, low], axis=-1).astype(jnp.bfloat16)


def join3(pieces):
    pieces = pieces.astype(jnp.float32)
    return (pieces[..., 0] + pieces[..., 1]) + pieces[..., 2]


def gather_bank(value):
    value = lax.all_gather(value, "y", axis=0, tiled=True)
    return lax.all_gather(value, "z", axis=0, tiled=True)


def body(queries, passages, passage_home, candidates, positive):
    shards = lax.axis_size(BANK)
    me = lax.axis_index(BANK)
    query_rows, query_len, feature_dim = queries.shape
    listed = candidates.shape[1]
    holdings = passages.shape[0]
    entries = query_rows * listed
    capacity = 3 * entries // shards
    width = query_len * feature_dim
    tail = 128

    lists = jnp.concatenate([candidates, positive[:, None]], axis=1)
    group_candidates = gather_bank(lists)[:, :listed]
    group_queries = gather_bank(queries)

    storage = passage_home[group_candidates].reshape(shards, entries)
    mine = (storage // holdings) == me
    position = jnp.cumsum(mine.astype(jnp.int32), axis=1) - 1
    slot_ids = jnp.arange(capacity, dtype=jnp.int32)
    hit = mine[:, None, :] & (position[:, None, :] == slot_ids[None, :, None])
    entry_ids = jnp.arange(entries, dtype=jnp.int32)
    entry = jnp.sum(jnp.where(hit, entry_ids[None, None, :], 0), axis=2)
    local_slot = jnp.sum(jnp.where(hit, (storage % holdings)[:, None, :], 0), axis=2)
    source = jnp.arange(shards, dtype=jnp.int32)[:, None]
    query_index = (source * query_rows + entry // listed).reshape(-1)
    local_slot = local_slot.reshape(-1)

    passage_tiles = passages[local_slot]
    query_tiles = group_queries[query_index]
    scores = jnp.einsum(
        "sid,sjd->sij", query_tiles, passage_tiles, preferred_element_type=jnp.float32
    )
    maxima, weights = soft_terms(scores)
    token_basis = jnp.einsum(
        "sij,sjd->sid", weights, passage_tiles, preferred_element_type=jnp.float32
    ).astype(jnp.bfloat16)
    slot_similarity = split3(jnp.sum(maxima, axis=1)).reshape(shards, capacity * 3)
    payload = jnp.concatenate(
        [
            token_basis.reshape(shards, capacity * width),
            slot_similarity,
            jnp.zeros((shards, tail - capacity * 3), jnp.bfloat16),
        ],
        axis=1,
    )
    returned = lax.all_to_all(payload, BANK, 0, 0, tiled=True)

    own_storage = passage_home[candidates].reshape(entries)
    holder = own_storage // holdings
    member = holder[:, None] == jnp.arange(shards, dtype=jnp.int32)[None, :]
    member = member.astype(jnp.int32)
    own_position = jnp.sum((jnp.cumsum(member, axis=0) - member) * member, axis=1)
    pieces = returned[:, capacity * width : capacity * width + capacity * 3]
    pieces = pieces.reshape(shards * capacity, 3)
    flat_slot = holder * capacity + own_position
    similarity = join3(pieces[flat_slot]).reshape(query_rows, listed)
    losses, coefficients = contrast(similarity, positive)
    slot_of = flat_slot.reshape(query_rows, listed)
    spread = jnp.arange(shards * capacity, dtype=jnp.int32)[None, None, :] == slot_of[:, :, None]
    spread = jnp.sum(
        jnp.where(spread, coefficients[:, :, None].astype(jnp.float32), 0.0), axis=1
    ).astype(jnp.bfloat16)
    bases = returned[:, : capacity * width].reshape(shards * capacity, width)
    gradient = jnp.einsum("qs,sd->qd", spread, bases, preferred_element_type=jnp.float32)
    return (losses, gradient.reshape(query_rows, query_len, feature_dim))


def solution(mesh):
    rows = mesh.shape["query"]
    bank = mesh.shape["bank"]
    across = 4 if bank % 4 == 0 else 1
    devices = np.asarray(mesh.devices).reshape(rows, bank // across, across)
    split_mesh = Mesh(devices, ("query",) + BANK)
    every = ("query",) + BANK
    return jax.shard_map(
        body,
        mesh=split_mesh,
        in_specs=(
            P(every, None, None),
            P(BANK, None, None),
            P(),
            P(every, None),
            P(every),
        ),
        out_specs=(P(every), P(every, None, None)),
        check_vma=False,
    )
```

```python
import functools

import jax
import jax.numpy as jnp
import numpy as np
from jax import lax
from jax.experimental import pallas as pl
from jax.experimental.pallas import tpu as pltpu
from jax.sharding import Mesh
from jax.sharding import PartitionSpec as P

BANK = ("z", "y")


def contrast(similarity, positive):
    largest = jnp.max(similarity, axis=1, keepdims=True)
    raised = jnp.exp(similarity - largest)
    totals = jnp.sum(raised, axis=1, keepdims=True)
    picked = jnp.arange(similarity.shape[1], dtype=jnp.int32)[None, :] == positive[:, None]
    losses = (
        largest[:, 0] + jnp.log(totals[:, 0]) - jnp.sum(jnp.where(picked, similarity, 0.0), axis=1)
    )
    coefficients = (raised / totals - picked.astype(jnp.float32)).astype(jnp.bfloat16)
    return (losses, coefficients)


def join3(pieces):
    pieces = pieces.astype(jnp.float32)
    return (pieces[..., 0] + pieces[..., 1]) + pieces[..., 2]


def gather_bank(value):
    value = lax.all_gather(value, "y", axis=0, tiled=True)
    return lax.all_gather(value, "z", axis=0, tiled=True)


def holder_kernel(capacity, slots_ref, picks_ref, queries_ref, *refs):
    tiles, out_ref = refs[:capacity], refs[capacity]
    source = pl.program_id(0)
    query_len, feature_dim = out_ref.shape[2], out_ref.shape[3]
    lane = lax.broadcasted_iota(jnp.int32, (1, feature_dim), 1)
    row = jnp.zeros((1, feature_dim), jnp.float32)
    for p in range(capacity):
        pick = picks_ref[source * capacity + p]
        query = queries_ref[pick]
        tile = tiles[p][0]
        scores = lax.dot_general(
            query, tile, (((1,), (1,)), ((), ())), preferred_element_type=jnp.float32
        )
        largest = jnp.max(scores, axis=1, keepdims=True)
        raised = jnp.exp(scores - largest)
        totals = jnp.sum(raised, axis=1, keepdims=True)
        maxima = largest + jnp.log(totals)
        weights = (raised / totals).astype(jnp.bfloat16)
        basis = jnp.dot(weights, tile, preferred_element_type=jnp.float32)
        out_ref[0, p] = basis.astype(jnp.bfloat16)
        similarity = jnp.sum(maxima, axis=0, keepdims=True)
        high = similarity.astype(jnp.bfloat16).astype(jnp.float32)
        rest = similarity - high
        middle = rest.astype(jnp.bfloat16).astype(jnp.float32)
        low = rest - middle
        row = jnp.where(lane == 3 * p, high, row)
        row = jnp.where(lane == 3 * p + 1, middle, row)
        row = jnp.where(lane == 3 * p + 2, low, row)
    sublane = lax.broadcasted_iota(jnp.int32, (query_len, feature_dim), 0)
    out_ref[0, capacity] = jnp.where(sublane == 0, row, 0.0).astype(jnp.bfloat16)


def holder_terms(slots, picks, group_queries, passages, shards, capacity):
    query_rows = group_queries.shape[0] // shards
    query_len, feature_dim = group_queries.shape[1], group_queries.shape[2]
    tile_len = passages.shape[1]

    def tile_spec(p):
        return pl.BlockSpec(
            (1, tile_len, feature_dim), lambda s, sl, pk: (sl[s * capacity + p], 0, 0)
        )

    grid_spec = pltpu.PrefetchScalarGridSpec(
        num_scalar_prefetch=2,
        grid=(shards,),
        in_specs=[pl.BlockSpec((query_rows, query_len, feature_dim), lambda s, sl, pk: (s, 0, 0))]
        + [tile_spec(p) for p in range(capacity)],
        out_specs=pl.BlockSpec(
            (1, capacity + 1, query_len, feature_dim), lambda s, sl, pk: (s, 0, 0, 0)
        ),
    )
    slots_total = shards * capacity
    flops = slots_total * 4 * query_len * tile_len * feature_dim
    moved = slots_total * (tile_len + query_len) * feature_dim * 2
    return pl.pallas_call(
        functools.partial(holder_kernel, capacity),
        grid_spec=grid_spec,
        out_shape=jax.ShapeDtypeStruct(
            (shards, capacity + 1, query_len, feature_dim), jnp.bfloat16
        ),
        cost_estimate=pl.CostEstimate(
            flops=flops, transcendentals=slots_total * query_len * tile_len, bytes_accessed=moved
        ),
    )(slots, picks, group_queries, *([passages] * capacity))


def body(queries, passages, passage_home, candidates, positive):
    shards = lax.axis_size(BANK)
    me = lax.axis_index(BANK)
    query_rows, query_len, feature_dim = queries.shape
    listed = candidates.shape[1]
    holdings = passages.shape[0]
    entries = query_rows * listed
    capacity = 3 * entries // shards
    width = query_len * feature_dim
    tail = 128

    own_storage = passage_home[candidates]
    holder = own_storage // holdings
    codes = jnp.concatenate(
        [holder, own_storage % holdings, jnp.zeros((query_rows, tail - 2 * listed), jnp.int32)],
        axis=1,
    ).astype(jnp.bfloat16)
    combined = jnp.concatenate([queries.reshape(query_rows, width), codes], axis=1)
    combined = gather_bank(combined)
    group_queries = combined[:, :width].reshape(shards * query_rows, query_len, feature_dim)
    group_codes = combined[:, width : width + 2 * listed].astype(jnp.int32)

    owner_bank = group_codes[:, :listed].reshape(shards, entries)
    stored_at = group_codes[:, listed:].reshape(shards, entries)
    mine = owner_bank == me
    position = jnp.cumsum(mine.astype(jnp.int32), axis=1) - 1
    slot_ids = jnp.arange(capacity, dtype=jnp.int32)
    hit = mine[:, None, :] & (position[:, None, :] == slot_ids[None, :, None])
    entry_ids = jnp.arange(entries, dtype=jnp.int32)
    entry = jnp.sum(jnp.where(hit, entry_ids[None, None, :], 0), axis=2)
    local_slot = jnp.sum(jnp.where(hit, stored_at[:, None, :], 0), axis=2)
    picks = (entry // listed).reshape(-1)
    payload = holder_terms(
        local_slot.reshape(-1), picks, group_queries, passages, shards, capacity
    )
    returned = lax.all_to_all(payload, BANK, 0, 0, tiled=True)

    holder = holder.reshape(entries)
    member = holder[:, None] == jnp.arange(shards, dtype=jnp.int32)[None, :]
    member = member.astype(jnp.int32)
    own_position = jnp.sum((jnp.cumsum(member, axis=0) - member) * member, axis=1)
    pieces = returned[:, capacity, 0, : capacity * 3].reshape(shards * capacity, 3)
    flat_slot = holder * capacity + own_position
    similarity = join3(pieces[flat_slot]).reshape(query_rows, listed)
    losses, coefficients = contrast(similarity, positive)
    slot_of = (holder * (capacity + 1) + own_position).reshape(query_rows, listed)
    rows = shards * (capacity + 1)
    spread = jnp.arange(rows, dtype=jnp.int32)[None, None, :] == slot_of[:, :, None]
    spread = jnp.sum(
        jnp.where(spread, coefficients[:, :, None].astype(jnp.float32), 0.0), axis=1
    ).astype(jnp.bfloat16)
    bases = returned.reshape(rows, query_len, feature_dim)
    gradient = jnp.einsum("qr,rid->qid", spread, bases, preferred_element_type=jnp.float32)
    return (losses, gradient)


def solution(mesh):
    rows = mesh.shape["query"]
    bank = mesh.shape["bank"]
    across = 4 if bank % 4 == 0 else 1
    devices = np.asarray(mesh.devices).reshape(rows, bank // across, across)
    split_mesh = Mesh(devices, ("query",) + BANK)
    every = ("query",) + BANK
    return jax.shard_map(
        body,
        mesh=split_mesh,
        in_specs=(
            P(every, None, None),
            P(BANK, None, None),
            P(),
            P(every, None),
            P(every),
        ),
        out_specs=(P(every), P(every, None, None)),
        check_vma=False,
    )
```

```python
import functools

import jax
import jax.numpy as jnp
import numpy as np
from jax import lax
from jax.experimental import pallas as pl
from jax.experimental.pallas import tpu as pltpu
from jax.sharding import Mesh
from jax.sharding import PartitionSpec as P

BANK = ("z", "y")


def contrast(similarity, positive):
    largest = jnp.max(similarity, axis=1, keepdims=True)
    raised = jnp.exp(similarity - largest)
    totals = jnp.sum(raised, axis=1, keepdims=True)
    picked = jnp.arange(similarity.shape[1], dtype=jnp.int32)[None, :] == positive[:, None]
    losses = (
        largest[:, 0] + jnp.log(totals[:, 0]) - jnp.sum(jnp.where(picked, similarity, 0.0), axis=1)
    )
    coefficients = (raised / totals - picked.astype(jnp.float32)).astype(jnp.bfloat16)
    return (losses, coefficients)


def join3(pieces):
    pieces = pieces.astype(jnp.float32)
    return (pieces[..., 0] + pieces[..., 1]) + pieces[..., 2]


def gather_bank(value):
    value = lax.all_gather(value, "y", axis=0, tiled=True)
    return lax.all_gather(value, "z", axis=0, tiled=True)


def holder_kernel(capacity, group, slots_ref, picks_ref, queries_ref, *refs):
    tiles, (out_ref, scores_ref, weights_ref) = refs[:capacity], refs[capacity:]
    source = pl.program_id(0)
    query_rows, query_len, feature_dim = queries_ref.shape
    tile_len = tiles[0].shape[1]

    @pl.when(source == 0)
    def _():
        weights_ref[...] = jnp.zeros_like(weights_ref)

    stacked = jnp.concatenate([tiles[p][0] for p in range(capacity)], axis=0)
    block = queries_ref[...].reshape(query_rows * query_len, feature_dim)
    scores_ref[...] = lax.dot_general(
        block, stacked, (((1,), (1,)), ((), ())), preferred_element_type=jnp.float32
    )
    lane = lax.broadcasted_iota(jnp.int32, (1, feature_dim), 1)
    row = jnp.zeros((1, feature_dim), jnp.float32)
    for p in range(capacity):
        pick = picks_ref[source * capacity + p]
        first = pl.multiple_of(pick * query_len, query_len)
        scores = scores_ref[pl.ds(first, query_len), pl.ds(p * tile_len, tile_len)]
        largest = jnp.max(scores, axis=1, keepdims=True)
        raised = jnp.exp(scores - largest)
        totals = jnp.sum(raised, axis=1, keepdims=True)
        maxima = largest + jnp.log(totals)
        g, r = p // group, p % group
        weights_ref[g, r * query_len : (r + 1) * query_len, r * tile_len : (r + 1) * tile_len] = (
            raised / totals
        ).astype(jnp.bfloat16)
        similarity = jnp.sum(maxima, axis=0, keepdims=True)
        high = similarity.astype(jnp.bfloat16).astype(jnp.float32)
        rest = similarity - high
        middle = rest.astype(jnp.bfloat16).astype(jnp.float32)
        low = rest - middle
        row = jnp.where(lane == 3 * p, high, row)
        row = jnp.where(lane == 3 * p + 1, middle, row)
        row = jnp.where(lane == 3 * p + 2, low, row)
    for g in range(capacity // group):
        basis = jnp.dot(
            weights_ref[g],
            stacked[g * group * tile_len : (g + 1) * group * tile_len],
            preferred_element_type=jnp.float32,
        )
        out_ref[0, g * group : (g + 1) * group] = basis.astype(jnp.bfloat16).reshape(
            group, query_len, feature_dim
        )
    sublane = lax.broadcasted_iota(jnp.int32, (query_len, feature_dim), 0)
    out_ref[0, capacity] = jnp.where(sublane == 0, row, 0.0).astype(jnp.bfloat16)


def holder_terms(slots, picks, group_queries, passages, shards, capacity):
    query_rows = group_queries.shape[0] // shards
    query_len, feature_dim = group_queries.shape[1], group_queries.shape[2]
    tile_len = passages.shape[1]

    def tile_spec(p):
        return pl.BlockSpec(
            (1, tile_len, feature_dim), lambda s, sl, pk: (sl[s * capacity + p], 0, 0)
        )

    group = 4 if capacity % 4 == 0 else 1
    grid_spec = pltpu.PrefetchScalarGridSpec(
        num_scalar_prefetch=2,
        grid=(shards,),
        in_specs=[pl.BlockSpec((query_rows, query_len, feature_dim), lambda s, sl, pk: (s, 0, 0))]
        + [tile_spec(p) for p in range(capacity)],
        out_specs=pl.BlockSpec(
            (1, capacity + 1, query_len, feature_dim), lambda s, sl, pk: (s, 0, 0, 0)
        ),
        scratch_shapes=[
            pltpu.VMEM((query_rows * query_len, capacity * tile_len), jnp.float32),
            pltpu.VMEM((capacity // group, group * query_len, group * tile_len), jnp.bfloat16),
        ],
    )
    slots_total = shards * capacity
    flops = shards * 2 * feature_dim * capacity * tile_len * (query_rows * query_len + group * query_len)
    moved = slots_total * (tile_len + query_len) * feature_dim * 2
    return pl.pallas_call(
        functools.partial(holder_kernel, capacity, group),
        grid_spec=grid_spec,
        out_shape=jax.ShapeDtypeStruct(
            (shards, capacity + 1, query_len, feature_dim), jnp.bfloat16
        ),
        cost_estimate=pl.CostEstimate(
            flops=flops, transcendentals=slots_total * query_len * tile_len, bytes_accessed=moved
        ),
    )(slots, picks, group_queries, *([passages] * capacity))


def body(queries, passages, passage_home, candidates, positive):
    shards = lax.axis_size(BANK)
    me = lax.axis_index(BANK)
    query_rows, query_len, feature_dim = queries.shape
    listed = candidates.shape[1]
    holdings = passages.shape[0]
    entries = query_rows * listed
    capacity = 3 * entries // shards
    width = query_len * feature_dim
    tail = 128

    own_storage = passage_home[candidates]
    holder = own_storage // holdings
    codes = jnp.concatenate(
        [holder, own_storage % holdings, jnp.zeros((query_rows, tail - 2 * listed), jnp.int32)],
        axis=1,
    ).astype(jnp.bfloat16)
    combined = jnp.concatenate([queries.reshape(query_rows, width), codes], axis=1)
    combined = gather_bank(combined)
    group_queries = combined[:, :width].reshape(shards * query_rows, query_len, feature_dim)
    group_codes = combined[:, width : width + 2 * listed].astype(jnp.int32)

    owner_bank = group_codes[:, :listed].reshape(shards, entries)
    stored_at = group_codes[:, listed:].reshape(shards, entries)
    mine = owner_bank == me
    position = jnp.cumsum(mine.astype(jnp.int32), axis=1) - 1
    slot_ids = jnp.arange(capacity, dtype=jnp.int32)
    hit = mine[:, None, :] & (position[:, None, :] == slot_ids[None, :, None])
    entry_ids = jnp.arange(entries, dtype=jnp.int32)
    entry = jnp.sum(jnp.where(hit, entry_ids[None, None, :], 0), axis=2)
    local_slot = jnp.sum(jnp.where(hit, stored_at[:, None, :], 0), axis=2)
    picks = (entry // listed).reshape(-1)
    payload = holder_terms(
        local_slot.reshape(-1), picks, group_queries, passages, shards, capacity
    )
    returned = lax.all_to_all(payload, BANK, 0, 0, tiled=True)

    holder = holder.reshape(entries)
    member = holder[:, None] == jnp.arange(shards, dtype=jnp.int32)[None, :]
    member = member.astype(jnp.int32)
    own_position = jnp.sum((jnp.cumsum(member, axis=0) - member) * member, axis=1)
    pieces = returned[:, capacity, 0, : capacity * 3].reshape(shards * capacity, 3)
    flat_slot = holder * capacity + own_position
    similarity = join3(pieces[flat_slot]).reshape(query_rows, listed)
    losses, coefficients = contrast(similarity, positive)
    slot_of = (holder * (capacity + 1) + own_position).reshape(query_rows, listed)
    rows = shards * (capacity + 1)
    spread = jnp.arange(rows, dtype=jnp.int32)[None, None, :] == slot_of[:, :, None]
    spread = jnp.sum(
        jnp.where(spread, coefficients[:, :, None].astype(jnp.float32), 0.0), axis=1
    ).astype(jnp.bfloat16)
    bases = returned.reshape(rows, query_len, feature_dim)
    gradient = jnp.einsum("qr,rid->qid", spread, bases, preferred_element_type=jnp.float32)
    return (losses, gradient)


def solution(mesh):
    rows = mesh.shape["query"]
    bank = mesh.shape["bank"]
    across = 4 if bank % 4 == 0 else 1
    devices = np.asarray(mesh.devices).reshape(rows, bank // across, across)
    split_mesh = Mesh(devices, ("query",) + BANK)
    every = ("query",) + BANK
    return jax.shard_map(
        body,
        mesh=split_mesh,
        in_specs=(
            P(every, None, None),
            P(BANK, None, None),
            P(),
            P(every, None),
            P(every),
        ),
        out_specs=(P(every), P(every, None, None)),
        check_vma=False,
    )
```

```python
import functools

import jax
import jax.numpy as jnp
import numpy as np
from jax import lax
from jax.experimental import pallas as pl
from jax.experimental.pallas import tpu as pltpu
from jax.sharding import Mesh
from jax.sharding import PartitionSpec as P

BANK = ("z", "y")


def contrast(similarity, positive):
    largest = jnp.max(similarity, axis=1, keepdims=True)
    raised = jnp.exp(similarity - largest)
    totals = jnp.sum(raised, axis=1, keepdims=True)
    picked = jnp.arange(similarity.shape[1], dtype=jnp.int32)[None, :] == positive[:, None]
    losses = (
        largest[:, 0] + jnp.log(totals[:, 0]) - jnp.sum(jnp.where(picked, similarity, 0.0), axis=1)
    )
    coefficients = (raised / totals - picked.astype(jnp.float32)).astype(jnp.bfloat16)
    return (losses, coefficients)


def join3(pieces):
    pieces = pieces.astype(jnp.float32)
    return (pieces[..., 0] + pieces[..., 1]) + pieces[..., 2]


def ring_gather(value, axis, size):
    def shift(x, step):
        return lax.ppermute(x, axis, [(i, (i + step) % size) for i in range(size)])

    right, left = [value], [value]
    for _ in range(size // 2):
        right.append(shift(right[-1], 1))
    for _ in range((size - 1) // 2):
        left.append(shift(left[-1], -1))
    return jnp.stack(right + left[1:][::-1], axis=0)


def gather_bank(value, shape):
    value = ring_gather(value, "y", shape[1])
    return ring_gather(value, "z", shape[0])


def holder_kernel(capacity, group, slots_ref, picks_ref, sources_ref, queries_ref, *refs):
    tiles, (out_ref, scores_ref, weights_ref) = refs[:capacity], refs[capacity:]
    source = pl.program_id(0)
    query_rows, query_len, feature_dim = queries_ref.shape
    tile_len = tiles[0].shape[1]

    @pl.when(source == 0)
    def _():
        weights_ref[...] = jnp.zeros_like(weights_ref)

    stacked = jnp.concatenate([tiles[p][0] for p in range(capacity)], axis=0)
    block = queries_ref[...].reshape(query_rows * query_len, feature_dim)
    scores_ref[...] = lax.dot_general(
        block, stacked, (((1,), (1,)), ((), ())), preferred_element_type=jnp.float32
    )
    lane = lax.broadcasted_iota(jnp.int32, (1, feature_dim), 1)
    row = jnp.zeros((1, feature_dim), jnp.float32)
    for p in range(capacity):
        pick = picks_ref[source * capacity + p]
        first = pl.multiple_of(pick * query_len, query_len)
        scores = scores_ref[pl.ds(first, query_len), pl.ds(p * tile_len, tile_len)]
        largest = jnp.max(scores, axis=1, keepdims=True)
        raised = jnp.exp(scores - largest)
        totals = jnp.sum(raised, axis=1, keepdims=True)
        maxima = largest + jnp.log(totals)
        g, r = p // group, p % group
        weights_ref[g, r * query_len : (r + 1) * query_len, r * tile_len : (r + 1) * tile_len] = (
            raised / totals
        ).astype(jnp.bfloat16)
        similarity = jnp.sum(maxima, axis=0, keepdims=True)
        high = similarity.astype(jnp.bfloat16).astype(jnp.float32)
        rest = similarity - high
        middle = rest.astype(jnp.bfloat16).astype(jnp.float32)
        low = rest - middle
        row = jnp.where(lane == 3 * p, high, row)
        row = jnp.where(lane == 3 * p + 1, middle, row)
        row = jnp.where(lane == 3 * p + 2, low, row)
    for g in range(capacity // group):
        basis = jnp.dot(
            weights_ref[g],
            stacked[g * group * tile_len : (g + 1) * group * tile_len],
            preferred_element_type=jnp.float32,
        )
        out_ref[0, g * group : (g + 1) * group] = basis.astype(jnp.bfloat16).reshape(
            group, query_len, feature_dim
        )
    sublane = lax.broadcasted_iota(jnp.int32, (query_len, feature_dim), 0)
    out_ref[0, capacity] = jnp.where(sublane == 0, row, 0.0).astype(jnp.bfloat16)


def holder_terms(slots, picks, sources, group_queries, passages, shards, capacity):
    query_rows = group_queries.shape[0] // shards
    query_len, feature_dim = group_queries.shape[1], group_queries.shape[2]
    tile_len = passages.shape[1]

    def tile_spec(p):
        return pl.BlockSpec(
            (1, tile_len, feature_dim), lambda s, sl, pk, sr: (sl[s * capacity + p], 0, 0)
        )

    group = 4 if capacity % 4 == 0 else 1
    grid_spec = pltpu.PrefetchScalarGridSpec(
        num_scalar_prefetch=3,
        grid=(shards,),
        in_specs=[pl.BlockSpec((query_rows, query_len, feature_dim), lambda s, sl, pk, sr: (s, 0, 0))]
        + [tile_spec(p) for p in range(capacity)],
        out_specs=pl.BlockSpec(
            (1, capacity + 1, query_len, feature_dim), lambda s, sl, pk, sr: (sr[s], 0, 0, 0)
        ),
        scratch_shapes=[
            pltpu.VMEM((query_rows * query_len, capacity * tile_len), jnp.float32),
            pltpu.VMEM((capacity // group, group * query_len, group * tile_len), jnp.bfloat16),
        ],
    )
    slots_total = shards * capacity
    flops = shards * 2 * feature_dim * capacity * tile_len * (query_rows * query_len + group * query_len)
    moved = slots_total * (tile_len + query_len) * feature_dim * 2
    return pl.pallas_call(
        functools.partial(holder_kernel, capacity, group),
        grid_spec=grid_spec,
        out_shape=jax.ShapeDtypeStruct(
            (shards, capacity + 1, query_len, feature_dim), jnp.bfloat16
        ),
        cost_estimate=pl.CostEstimate(
            flops=flops, transcendentals=slots_total * query_len * tile_len, bytes_accessed=moved
        ),
    )(slots, picks, sources, group_queries, *([passages] * capacity))


def body(queries, passages, passage_home, candidates, positive):
    shards = lax.axis_size(BANK)
    me = lax.axis_index(BANK)
    query_rows, query_len, feature_dim = queries.shape
    listed = candidates.shape[1]
    holdings = passages.shape[0]
    entries = query_rows * listed
    capacity = 3 * entries // shards
    width = query_len * feature_dim
    tail = 128

    own_storage = passage_home[candidates]
    holder = own_storage // holdings
    codes = jnp.concatenate(
        [holder, own_storage % holdings, jnp.zeros((query_rows, tail - 2 * listed), jnp.int32)],
        axis=1,
    ).astype(jnp.bfloat16)
    combined = jnp.concatenate([queries.reshape(query_rows, width), codes], axis=1)
    spans = (lax.axis_size("z"), lax.axis_size("y"))
    combined = gather_bank(combined, spans).reshape(shards * query_rows, -1)
    offset_z = jnp.arange(spans[0], dtype=jnp.int32)[:, None]
    offset_y = jnp.arange(spans[1], dtype=jnp.int32)[None, :]
    sources = (
        (lax.axis_index("z") - offset_z) % spans[0] * spans[1]
        + (lax.axis_index("y") - offset_y) % spans[1]
    ).reshape(shards)
    group_queries = combined[:, :width].reshape(shards * query_rows, query_len, feature_dim)
    group_codes = combined[:, width : width + 2 * listed].astype(jnp.int32)

    owner_bank = group_codes[:, :listed].reshape(shards, entries)
    stored_at = group_codes[:, listed:].reshape(shards, entries)
    mine = owner_bank == me
    position = jnp.cumsum(mine.astype(jnp.int32), axis=1) - 1
    slot_ids = jnp.arange(capacity, dtype=jnp.int32)
    hit = mine[:, None, :] & (position[:, None, :] == slot_ids[None, :, None])
    entry_ids = jnp.arange(entries, dtype=jnp.int32)
    entry = jnp.sum(jnp.where(hit, entry_ids[None, None, :], 0), axis=2)
    local_slot = jnp.sum(jnp.where(hit, stored_at[:, None, :], 0), axis=2)
    picks = (entry // listed).reshape(-1)
    payload = holder_terms(
        local_slot.reshape(-1), picks, sources, group_queries, passages, shards, capacity
    )
    returned = lax.all_to_all(payload, BANK, 0, 0, tiled=True)

    holder = holder.reshape(entries)
    member = holder[:, None] == jnp.arange(shards, dtype=jnp.int32)[None, :]
    member = member.astype(jnp.int32)
    own_position = jnp.sum((jnp.cumsum(member, axis=0) - member) * member, axis=1)
    pieces = returned[:, capacity, 0, : capacity * 3].reshape(shards * capacity, 3)
    flat_slot = holder * capacity + own_position
    similarity = join3(pieces[flat_slot]).reshape(query_rows, listed)
    losses, coefficients = contrast(similarity, positive)
    slot_of = (holder * (capacity + 1) + own_position).reshape(query_rows, listed)
    rows = shards * (capacity + 1)
    spread = jnp.arange(rows, dtype=jnp.int32)[None, None, :] == slot_of[:, :, None]
    spread = jnp.sum(
        jnp.where(spread, coefficients[:, :, None].astype(jnp.float32), 0.0), axis=1
    ).astype(jnp.bfloat16)
    bases = returned.reshape(rows, query_len, feature_dim)
    gradient = jnp.einsum("qr,rid->qid", spread, bases, preferred_element_type=jnp.float32)
    return (losses, gradient)


def solution(mesh):
    rows = mesh.shape["query"]
    bank = mesh.shape["bank"]
    across = 4 if bank % 4 == 0 else 1
    devices = np.asarray(mesh.devices).reshape(rows, bank // across, across)
    split_mesh = Mesh(devices, ("query",) + BANK)
    every = ("query",) + BANK
    return jax.shard_map(
        body,
        mesh=split_mesh,
        in_specs=(
            P(every, None, None),
            P(BANK, None, None),
            P(),
            P(every, None),
            P(every),
        ),
        out_specs=(P(every), P(every, None, None)),
        check_vma=False,
    )
```

```python
import functools

import jax
import jax.numpy as jnp
import numpy as np
from jax import lax
from jax.experimental import pallas as pl
from jax.experimental.pallas import tpu as pltpu
from jax.sharding import Mesh
from jax.sharding import PartitionSpec as P


BANK = ("z", "y")


def contrast(similarity, positive):
    largest = jnp.max(similarity, axis=1, keepdims=True)
    raised = jnp.exp(similarity - largest)
    totals = jnp.sum(raised, axis=1, keepdims=True)
    picked = jnp.arange(similarity.shape[1], dtype=jnp.int32)[None, :] == positive[:, None]
    losses = (
        largest[:, 0] + jnp.log(totals[:, 0]) - jnp.sum(jnp.where(picked, similarity, 0.0), axis=1)
    )
    coefficients = (raised / totals - picked.astype(jnp.float32)).astype(jnp.bfloat16)
    return (losses, coefficients)


def join3(pieces):
    pieces = pieces.astype(jnp.float32)
    return (pieces[..., 0] + pieces[..., 1]) + pieces[..., 2]


def ring_gather(value, axis, size):
    def shift(x, step):
        return lax.ppermute(x, axis, [(i, (i + step) % size) for i in range(size)])

    right, left = [value], [value]
    for hop in range(size // 2):
        right.append(shift(right[-1], 1))
        if hop < (size - 1) // 2:
            left.append(shift(left[-1], -1))
    return right + left[1:][::-1]


def holder_kernel(capacity, group, slots_ref, picks_ref, sources_ref, queries_ref, *refs):
    tiles, (_, out_ref, scores_ref, weights_ref) = refs[:capacity], refs[capacity:]
    source = pl.program_id(0)
    query_rows, query_len, feature_dim = queries_ref.shape
    tile_len = tiles[0].shape[1]

    @pl.when(source == 0)
    def _():
        weights_ref[...] = jnp.zeros_like(weights_ref)

    stacked = jnp.concatenate([tiles[p][0] for p in range(capacity)], axis=0)
    block = queries_ref[...].reshape(query_rows * query_len, feature_dim)
    scores_ref[...] = lax.dot_general(
        block, stacked, (((1,), (1,)), ((), ())), preferred_element_type=jnp.float32
    )
    lane = lax.broadcasted_iota(jnp.int32, (1, feature_dim), 1)
    row = jnp.zeros((1, feature_dim), jnp.float32)
    for p in range(capacity):
        pick = picks_ref[source * capacity + p]
        first = pl.multiple_of(pick * query_len, query_len)
        scores = scores_ref[pl.ds(first, query_len), pl.ds(p * tile_len, tile_len)]
        largest = jnp.max(scores, axis=1, keepdims=True)
        raised = jnp.exp(scores - largest)
        totals = jnp.sum(raised, axis=1, keepdims=True)
        maxima = largest + jnp.log(totals)
        g, r = p // group, p % group
        weights_ref[g, r * query_len : (r + 1) * query_len, r * tile_len : (r + 1) * tile_len] = (
            raised / totals
        ).astype(jnp.bfloat16)
        similarity = jnp.sum(maxima, axis=0, keepdims=True)
        high = similarity.astype(jnp.bfloat16).astype(jnp.float32)
        rest = similarity - high
        middle = rest.astype(jnp.bfloat16).astype(jnp.float32)
        low = rest - middle
        row = jnp.where(lane == 3 * p, high, row)
        row = jnp.where(lane == 3 * p + 1, middle, row)
        row = jnp.where(lane == 3 * p + 2, low, row)
    for g in range(capacity // group):
        basis = jnp.dot(
            weights_ref[g],
            stacked[g * group * tile_len : (g + 1) * group * tile_len],
            preferred_element_type=jnp.float32,
        )
        out_ref[0, g * group : (g + 1) * group] = basis.astype(jnp.bfloat16).reshape(
            group, query_len, feature_dim
        )
    sublane = lax.broadcasted_iota(jnp.int32, (query_len, feature_dim), 0)
    out_ref[0, capacity] = jnp.where(sublane == 0, row, 0.0).astype(jnp.bfloat16)


def holder_terms(slots, picks, sources, group_queries, passages, payload, capacity):
    shards = sources.shape[0]
    query_rows = group_queries.shape[0] // shards
    query_len, feature_dim = group_queries.shape[1], group_queries.shape[2]
    tile_len = passages.shape[1]

    def tile_spec(p):
        return pl.BlockSpec(
            (1, tile_len, feature_dim), lambda s, sl, pk, sr: (sl[s * capacity + p], 0, 0)
        )

    group = 4 if capacity % 4 == 0 else 1
    grid_spec = pltpu.PrefetchScalarGridSpec(
        num_scalar_prefetch=3,
        grid=(shards,),
        in_specs=[pl.BlockSpec((query_rows, query_len, feature_dim), lambda s, sl, pk, sr: (s, 0, 0))]
        + [tile_spec(p) for p in range(capacity)]
        + [pl.BlockSpec(memory_space=pl.ANY)],
        out_specs=pl.BlockSpec(
            (1, capacity + 1, query_len, feature_dim), lambda s, sl, pk, sr: (sr[s], 0, 0, 0)
        ),
        scratch_shapes=[
            pltpu.VMEM((query_rows * query_len, capacity * tile_len), jnp.float32),
            pltpu.VMEM((capacity // group, group * query_len, group * tile_len), jnp.bfloat16),
        ],
    )
    slots_total = shards * capacity
    flops = shards * 2 * feature_dim * capacity * tile_len * (query_rows * query_len + group * query_len)
    moved = slots_total * (tile_len + query_len) * feature_dim * 2
    return pl.pallas_call(
        functools.partial(holder_kernel, capacity, group),
        grid_spec=grid_spec,
        out_shape=jax.ShapeDtypeStruct(payload.shape, payload.dtype),
        input_output_aliases={4 + capacity: 0},
        cost_estimate=pl.CostEstimate(
            flops=flops, transcendentals=slots_total * query_len * tile_len, bytes_accessed=moved
        ),
    )(slots, picks, sources, group_queries, *([passages] * capacity), payload)


def terms(queries, passages, passage_home, candidates, positive):
    shards = lax.axis_size(BANK)
    me = lax.axis_index(BANK)
    query_rows, query_len, feature_dim = queries.shape
    listed = candidates.shape[1]
    holdings = passages.shape[0]
    entries = query_rows * listed
    capacity = 3 * entries // shards
    width = query_len * feature_dim
    tail = 128

    own_storage = passage_home[candidates]
    holder = own_storage // holdings
    codes = jnp.concatenate(
        [holder, own_storage % holdings, jnp.zeros((query_rows, tail - 2 * listed), jnp.int32)],
        axis=1,
    ).astype(jnp.bfloat16)
    combined = jnp.concatenate([queries.reshape(query_rows, width), codes], axis=1)
    spans = (lax.axis_size("z"), lax.axis_size("y"))
    nearby = jnp.stack(ring_gather(combined, "y", spans[1]), axis=0)
    arrivals = ring_gather(nearby, "z", spans[0])
    offset_y = jnp.arange(spans[1], dtype=jnp.int32)
    near_sources = (lax.axis_index("y") - offset_y) % spans[1]
    payload = jnp.zeros((shards, capacity + 1, query_len, feature_dim), jnp.bfloat16)
    half = spans[0] // 2
    groups = [[0]] + [[d, spans[0] - d] for d in range(1, (spans[0] + 1) // 2)]
    if spans[0] % 2 == 0:
        groups.append([half])
    for offsets in groups:
        block = jnp.concatenate([arrivals[d] for d in offsets], axis=0)
        block, payload = lax.optimization_barrier((block, payload))
        count = len(offsets) * spans[1]
        block = block.reshape(count * query_rows, width + tail)
        group_queries = block[:, :width].reshape(count * query_rows, query_len, feature_dim)
        group_codes = block[:, width : width + 2 * listed].astype(jnp.int32)
        sources = jnp.concatenate(
            [(lax.axis_index("z") - d) % spans[0] * spans[1] + near_sources for d in offsets]
        )
        owner_bank = group_codes[:, :listed].reshape(count, entries)
        stored_at = group_codes[:, listed:].reshape(count, entries)
        mine = owner_bank == me
        position = jnp.cumsum(mine.astype(jnp.int32), axis=1) - 1
        slot_ids = jnp.arange(capacity, dtype=jnp.int32)
        hit = mine[:, None, :] & (position[:, None, :] == slot_ids[None, :, None])
        entry_ids = jnp.arange(entries, dtype=jnp.int32)
        entry = jnp.sum(jnp.where(hit, entry_ids[None, None, :], 0), axis=2)
        local_slot = jnp.sum(jnp.where(hit, stored_at[:, None, :], 0), axis=2)
        picks = (entry // listed).reshape(-1)
        payload = holder_terms(
            local_slot.reshape(-1), picks, sources, group_queries, passages, payload, capacity
        )
    returned = lax.all_to_all(payload, BANK, 0, 0, tiled=True)

    holder = holder.reshape(entries)
    member = holder[:, None] == jnp.arange(shards, dtype=jnp.int32)[None, :]
    member = member.astype(jnp.int32)
    own_position = jnp.sum((jnp.cumsum(member, axis=0) - member) * member, axis=1)
    pieces = returned[:, capacity, 0, : capacity * 3].reshape(shards * capacity, 3)
    flat_slot = holder * capacity + own_position
    similarity = join3(pieces[flat_slot]).reshape(query_rows, listed)
    losses, coefficients = contrast(similarity, positive)
    slot_of = (holder * (capacity + 1) + own_position).reshape(query_rows, listed)
    rows = shards * (capacity + 1)
    spread = jnp.arange(rows, dtype=jnp.int32)[None, None, :] == slot_of[:, :, None]
    spread = jnp.sum(
        jnp.where(spread, coefficients[:, :, None].astype(jnp.float32), 0.0), axis=1
    ).astype(jnp.bfloat16)
    bases = returned.reshape(rows, query_len, feature_dim)
    gradient = jnp.einsum("qr,rid->qid", spread, bases, preferred_element_type=jnp.float32)
    return (losses, gradient)


def solution(mesh):
    rows = mesh.shape["query"]
    bank = mesh.shape["bank"]
    across = 4 if bank % 4 == 0 else 1
    devices = np.asarray(mesh.devices).reshape(rows, bank // across, across)
    split_mesh = Mesh(devices, ("query",) + BANK)
    every = ("query",) + BANK
    return jax.shard_map(
        terms,
        mesh=split_mesh,
        in_specs=(
            P(every, None, None),
            P(BANK, None, None),
            P(),
            P(every, None),
            P(every),
        ),
        out_specs=(P(every), P(every, None, None)),
        check_vma=False,
    )
```

```python
import functools

import jax
import jax.numpy as jnp
import numpy as np
from jax import lax
from jax.experimental import pallas as pl
from jax.experimental.pallas import tpu as pltpu
from jax.sharding import Mesh
from jax.sharding import PartitionSpec as P

BANK = ("z", "y")


def contrast(similarity, positive):
    largest = jnp.max(similarity, axis=1, keepdims=True)
    raised = jnp.exp(similarity - largest)
    totals = jnp.sum(raised, axis=1, keepdims=True)
    picked = jnp.arange(similarity.shape[1], dtype=jnp.int32)[None, :] == positive[:, None]
    losses = (
        largest[:, 0] + jnp.log(totals[:, 0]) - jnp.sum(jnp.where(picked, similarity, 0.0), axis=1)
    )
    coefficients = (raised / totals - picked.astype(jnp.float32)).astype(jnp.bfloat16)
    return (losses, coefficients)


def join3(pieces):
    pieces = pieces.astype(jnp.float32)
    return (pieces[..., 0] + pieces[..., 1]) + pieces[..., 2]


def ring_gather(value, axis, size):
    def shift(x, step):
        return lax.ppermute(x, axis, [(i, (i + step) % size) for i in range(size)])

    right, left = [value], [value]
    for _ in range(size // 2):
        right.append(shift(right[-1], 1))
    for _ in range((size - 1) // 2):
        left.append(shift(left[-1], -1))
    return jnp.stack(right + left[1:][::-1], axis=0)


def gather_bank(value, shape):
    nearby = ring_gather(value, "y", shape[1])
    order = (lax.axis_index("y") - jnp.arange(shape[1], dtype=jnp.int32)) % shape[1]
    nearby = jnp.take(nearby, order, axis=0)
    return ring_gather(nearby, "z", shape[0])


def holder_kernel(capacity, group, per, slots_ref, picks_ref, sources_ref, queries_ref, *refs):
    tiles, (out_ref, scores_ref, weights_ref) = refs[: per * capacity], refs[per * capacity :]

    @pl.when(pl.program_id(0) == 0)
    def _():
        weights_ref[...] = jnp.zeros_like(weights_ref)

    for unit in range(per):
        source_terms(
            capacity, group, per, unit, picks_ref, queries_ref,
            tiles[unit * capacity : (unit + 1) * capacity], out_ref, scores_ref, weights_ref,
        )


def source_terms(capacity, group, per, unit, picks_ref, queries_ref, tiles, out_ref, scores_ref, weights_ref):
    source = pl.program_id(0) * per + unit
    query_rows = queries_ref.shape[0] // per
    query_len, feature_dim = queries_ref.shape[1], queries_ref.shape[2]
    tile_len = tiles[0].shape[1]
    stacked = jnp.concatenate([tiles[p][0] for p in range(capacity)], axis=0)
    block = queries_ref[unit * query_rows : (unit + 1) * query_rows].reshape(
        query_rows * query_len, feature_dim
    )
    scores_ref[...] = lax.dot_general(
        block, stacked, (((1,), (1,)), ((), ())), preferred_element_type=jnp.float32
    )
    lane = lax.broadcasted_iota(jnp.int32, (1, feature_dim), 1)
    row = jnp.zeros((1, feature_dim), jnp.float32)
    for p in range(capacity):
        pick = picks_ref[source * capacity + p]
        first = pl.multiple_of(pick * query_len, query_len)
        scores = scores_ref[pl.ds(first, query_len), pl.ds(p * tile_len, tile_len)]
        largest = jnp.max(scores, axis=1, keepdims=True)
        raised = jnp.exp(scores - largest)
        totals = jnp.sum(raised, axis=1, keepdims=True)
        maxima = largest + jnp.log(totals)
        g, r = p // group, p % group
        weights_ref[g, r * query_len : (r + 1) * query_len, r * tile_len : (r + 1) * tile_len] = (
            raised / totals
        ).astype(jnp.bfloat16)
        similarity = jnp.sum(maxima, axis=0, keepdims=True)
        high = similarity.astype(jnp.bfloat16).astype(jnp.float32)
        rest = similarity - high
        middle = rest.astype(jnp.bfloat16).astype(jnp.float32)
        low = rest - middle
        row = jnp.where(lane == 3 * p, high, row)
        row = jnp.where(lane == 3 * p + 1, middle, row)
        row = jnp.where(lane == 3 * p + 2, low, row)
    for g in range(capacity // group):
        basis = jnp.dot(
            weights_ref[g],
            stacked[g * group * tile_len : (g + 1) * group * tile_len],
            preferred_element_type=jnp.float32,
        )
        out_ref[unit, g * group : (g + 1) * group] = basis.astype(jnp.bfloat16).reshape(
            group, query_len, feature_dim
        )
    sublane = lax.broadcasted_iota(jnp.int32, (query_len, feature_dim), 0)
    out_ref[unit, capacity] = jnp.where(sublane == 0, row, 0.0).astype(jnp.bfloat16)


def holder_terms(slots, picks, sources, group_queries, passages, shards, capacity, per):
    query_rows = group_queries.shape[0] // shards
    steps = shards // per
    query_len, feature_dim = group_queries.shape[1], group_queries.shape[2]
    tile_len = passages.shape[1]

    def tile_spec(t):
        return pl.BlockSpec(
            (1, tile_len, feature_dim), lambda s, sl, pk, sr: (sl[s * per * capacity + t], 0, 0)
        )

    group = 4 if capacity % 4 == 0 else 1
    grid_spec = pltpu.PrefetchScalarGridSpec(
        num_scalar_prefetch=3,
        grid=(steps,),
        in_specs=[
            pl.BlockSpec((per * query_rows, query_len, feature_dim), lambda s, sl, pk, sr: (s, 0, 0))
        ]
        + [tile_spec(t) for t in range(per * capacity)],
        out_specs=pl.BlockSpec(
            (per, capacity + 1, query_len, feature_dim), lambda s, sl, pk, sr: (sr[s], 0, 0, 0)
        ),
        scratch_shapes=[
            pltpu.VMEM((query_rows * query_len, capacity * tile_len), jnp.float32),
            pltpu.VMEM((capacity // group, group * query_len, group * tile_len), jnp.bfloat16),
        ],
    )
    slots_total = shards * capacity
    flops = shards * 2 * feature_dim * capacity * tile_len * (query_rows * query_len + group * query_len)
    moved = slots_total * (tile_len + query_len) * feature_dim * 2
    return pl.pallas_call(
        functools.partial(holder_kernel, capacity, group, per),
        grid_spec=grid_spec,
        out_shape=jax.ShapeDtypeStruct(
            (shards, capacity + 1, query_len, feature_dim), jnp.bfloat16
        ),
        cost_estimate=pl.CostEstimate(
            flops=flops, transcendentals=slots_total * query_len * tile_len, bytes_accessed=moved
        ),
    )(slots, picks, sources, group_queries, *([passages] * (per * capacity)))


def body(queries, passages, passage_home, candidates, positive):
    shards = lax.axis_size(BANK)
    me = lax.axis_index(BANK)
    query_rows, query_len, feature_dim = queries.shape
    listed = candidates.shape[1]
    holdings = passages.shape[0]
    entries = query_rows * listed
    capacity = 3 * entries // shards
    width = query_len * feature_dim
    tail = 128

    own_storage = passage_home[candidates]
    holder = own_storage // holdings
    codes = jnp.concatenate(
        [holder, own_storage % holdings, jnp.zeros((query_rows, tail - 2 * listed), jnp.int32)],
        axis=1,
    ).astype(jnp.bfloat16)
    combined = jnp.concatenate([queries.reshape(query_rows, width), codes], axis=1)
    spans = (lax.axis_size("z"), lax.axis_size("y"))
    combined = gather_bank(combined, spans).reshape(shards * query_rows, -1)
    offset_z = jnp.arange(spans[0], dtype=jnp.int32)
    sources = (lax.axis_index("z") - offset_z) % spans[0]
    group_queries = combined[:, :width].reshape(shards * query_rows, query_len, feature_dim)
    group_codes = combined[:, width : width + 2 * listed].astype(jnp.int32)

    owner_bank = group_codes[:, :listed].reshape(shards, entries)
    stored_at = group_codes[:, listed:].reshape(shards, entries)
    mine = owner_bank == me
    position = jnp.cumsum(mine.astype(jnp.int32), axis=1) - 1
    slot_ids = jnp.arange(capacity, dtype=jnp.int32)
    hit = mine[:, None, :] & (position[:, None, :] == slot_ids[None, :, None])
    entry_ids = jnp.arange(entries, dtype=jnp.int32)
    entry = jnp.sum(jnp.where(hit, entry_ids[None, None, :], 0), axis=2)
    local_slot = jnp.sum(jnp.where(hit, stored_at[:, None, :], 0), axis=2)
    picks = (entry // listed).reshape(-1)
    payload = holder_terms(
        local_slot.reshape(-1), picks, sources, group_queries, passages, shards, capacity, spans[1]
    )
    returned = lax.all_to_all(payload, BANK, 0, 0, tiled=True)

    holder = holder.reshape(entries)
    member = holder[:, None] == jnp.arange(shards, dtype=jnp.int32)[None, :]
    member = member.astype(jnp.int32)
    own_position = jnp.sum((jnp.cumsum(member, axis=0) - member) * member, axis=1)
    pieces = returned[:, capacity, 0, : capacity * 3].reshape(shards * capacity, 3)
    flat_slot = holder * capacity + own_position
    similarity = join3(pieces[flat_slot]).reshape(query_rows, listed)
    losses, coefficients = contrast(similarity, positive)
    slot_of = (holder * (capacity + 1) + own_position).reshape(query_rows, listed)
    rows = shards * (capacity + 1)
    spread = jnp.arange(rows, dtype=jnp.int32)[None, None, :] == slot_of[:, :, None]
    spread = jnp.sum(
        jnp.where(spread, coefficients[:, :, None].astype(jnp.float32), 0.0), axis=1
    ).astype(jnp.bfloat16)
    bases = returned.reshape(rows, query_len, feature_dim)
    gradient = jnp.einsum("qr,rid->qid", spread, bases, preferred_element_type=jnp.float32)
    return (losses, gradient)


def solution(mesh):
    rows = mesh.shape["query"]
    bank = mesh.shape["bank"]
    across = 4 if bank % 4 == 0 else 1
    devices = np.asarray(mesh.devices).reshape(rows, bank // across, across)
    split_mesh = Mesh(devices, ("query",) + BANK)
    every = ("query",) + BANK
    return jax.shard_map(
        body,
        mesh=split_mesh,
        in_specs=(
            P(every, None, None),
            P(BANK, None, None),
            P(),
            P(every, None),
            P(every),
        ),
        out_specs=(P(every), P(every, None, None)),
        check_vma=False,
    )
```

```python
import functools

import jax
import jax.numpy as jnp
import numpy as np
from jax import lax
from jax.experimental import pallas as pl
from jax.experimental.pallas import tpu as pltpu
from jax.sharding import Mesh
from jax.sharding import PartitionSpec as P

BANK = ("z", "y")


def contrast(similarity, positive):
    largest = jnp.max(similarity, axis=1, keepdims=True)
    raised = jnp.exp(similarity - largest)
    totals = jnp.sum(raised, axis=1, keepdims=True)
    picked = jnp.arange(similarity.shape[1], dtype=jnp.int32)[None, :] == positive[:, None]
    losses = (
        largest[:, 0] + jnp.log(totals[:, 0]) - jnp.sum(jnp.where(picked, similarity, 0.0), axis=1)
    )
    coefficients = (raised / totals - picked.astype(jnp.float32)).astype(jnp.bfloat16)
    return (losses, coefficients)


def join3(pieces):
    pieces = pieces.astype(jnp.float32)
    return (pieces[..., 0] + pieces[..., 1]) + pieces[..., 2]


def ring_gather(value, axis, size):
    def shift(x, step):
        return lax.ppermute(x, axis, [(i, (i + step) % size) for i in range(size)])

    right, left = [value], [value]
    for _ in range(size // 2):
        right.append(shift(right[-1], 1))
    for _ in range((size - 1) // 2):
        left.append(shift(left[-1], -1))
    return jnp.stack(right + left[1:][::-1], axis=0)


def gather_bank(value, shape):
    nearby = ring_gather(value, "y", shape[1])
    order = (lax.axis_index("y") - jnp.arange(shape[1], dtype=jnp.int32)) % shape[1]
    nearby = jnp.take(nearby, order, axis=0)
    return ring_gather(nearby, "z", shape[0])


def holder_kernel(capacity, group, per, slots_ref, picks_ref, sources_ref, queries_ref, *refs):
    tiles, (out_ref, scores_ref, weights_ref) = refs[: per * capacity], refs[per * capacity :]

    @pl.when(pl.program_id(0) == 0)
    def _():
        weights_ref[...] = jnp.zeros_like(weights_ref)

    for unit in range(per):
        source_terms(
            capacity, group, per, unit, picks_ref, queries_ref,
            tiles[unit * capacity : (unit + 1) * capacity], out_ref, scores_ref, weights_ref,
        )


def source_terms(capacity, group, per, unit, picks_ref, queries_ref, tiles, out_ref, scores_ref, weights_ref):
    source = pl.program_id(0) * per + unit
    query_rows = queries_ref.shape[0] // per
    query_len, feature_dim = queries_ref.shape[1], queries_ref.shape[2]
    tile_len = tiles[0].shape[1]
    stacked = jnp.concatenate([tiles[p][0] for p in range(capacity)], axis=0)
    block = queries_ref[unit * query_rows : (unit + 1) * query_rows].reshape(
        query_rows * query_len, feature_dim
    )
    scores_ref[...] = lax.dot_general(
        block, stacked, (((1,), (1,)), ((), ())), preferred_element_type=jnp.float32
    )
    lane = lax.broadcasted_iota(jnp.int32, (1, feature_dim), 1)
    row = jnp.zeros((1, feature_dim), jnp.float32)
    for p in range(capacity):
        pick = picks_ref[source * capacity + p]
        first = pl.multiple_of(pick * query_len, query_len)
        scores = scores_ref[pl.ds(first, query_len), pl.ds(p * tile_len, tile_len)]
        largest = jnp.max(scores, axis=1, keepdims=True)
        raised = jnp.exp(scores - largest)
        totals = jnp.sum(raised, axis=1, keepdims=True)
        maxima = largest + jnp.log(totals)
        g, r = p // group, p % group
        weights_ref[g, r * query_len : (r + 1) * query_len, r * tile_len : (r + 1) * tile_len] = (
            raised / totals
        ).astype(jnp.bfloat16)
        similarity = jnp.sum(maxima, axis=0, keepdims=True)
        high = similarity.astype(jnp.bfloat16).astype(jnp.float32)
        rest = similarity - high
        middle = rest.astype(jnp.bfloat16).astype(jnp.float32)
        low = rest - middle
        row = jnp.where(lane == 3 * p, high, row)
        row = jnp.where(lane == 3 * p + 1, middle, row)
        row = jnp.where(lane == 3 * p + 2, low, row)
    for g in range(capacity // group):
        basis = jnp.dot(
            weights_ref[g],
            stacked[g * group * tile_len : (g + 1) * group * tile_len],
            preferred_element_type=jnp.float32,
        )
        out_ref[unit, g * group : (g + 1) * group] = basis.astype(jnp.bfloat16).reshape(
            group, query_len, feature_dim
        )
    sublane = lax.broadcasted_iota(jnp.int32, (query_len, feature_dim), 0)
    out_ref[unit, capacity] = jnp.where(sublane == 0, row, 0.0).astype(jnp.bfloat16)


def holder_terms(slots, picks, sources, group_queries, passages, shards, capacity, per):
    query_rows = group_queries.shape[0] // shards
    steps = shards // per
    query_len, feature_dim = group_queries.shape[1], group_queries.shape[2]
    tile_len = passages.shape[1]

    def tile_spec(t):
        return pl.BlockSpec(
            (1, tile_len, feature_dim), lambda s, sl, pk, sr: (sl[s * per * capacity + t], 0, 0)
        )

    group = 2 if capacity % 2 == 0 else 1
    grid_spec = pltpu.PrefetchScalarGridSpec(
        num_scalar_prefetch=3,
        grid=(steps,),
        in_specs=[
            pl.BlockSpec((per * query_rows, query_len, feature_dim), lambda s, sl, pk, sr: (s, 0, 0))
        ]
        + [tile_spec(t) for t in range(per * capacity)],
        out_specs=pl.BlockSpec(
            (per, capacity + 1, query_len, feature_dim), lambda s, sl, pk, sr: (sr[s], 0, 0, 0)
        ),
        scratch_shapes=[
            pltpu.VMEM((query_rows * query_len, capacity * tile_len), jnp.float32),
            pltpu.VMEM((capacity // group, group * query_len, group * tile_len), jnp.bfloat16),
        ],
    )
    slots_total = shards * capacity
    flops = shards * 2 * feature_dim * capacity * tile_len * (query_rows * query_len + group * query_len)
    moved = slots_total * (tile_len + query_len) * feature_dim * 2
    return pl.pallas_call(
        functools.partial(holder_kernel, capacity, group, per),
        grid_spec=grid_spec,
        out_shape=jax.ShapeDtypeStruct(
            (shards, capacity + 1, query_len, feature_dim), jnp.bfloat16
        ),
        cost_estimate=pl.CostEstimate(
            flops=flops, transcendentals=slots_total * query_len * tile_len, bytes_accessed=moved
        ),
    )(slots, picks, sources, group_queries, *([passages] * (per * capacity)))


def body(queries, passages, passage_home, candidates, positive):
    shards = lax.axis_size(BANK)
    me = lax.axis_index(BANK)
    query_rows, query_len, feature_dim = queries.shape
    listed = candidates.shape[1]
    holdings = passages.shape[0]
    entries = query_rows * listed
    capacity = 3 * entries // shards
    width = query_len * feature_dim
    tail = 128

    own_storage = passage_home[candidates]
    holder = own_storage // holdings
    codes = jnp.concatenate(
        [holder, own_storage % holdings, jnp.zeros((query_rows, tail - 2 * listed), jnp.int32)],
        axis=1,
    ).astype(jnp.bfloat16)
    combined = jnp.concatenate([queries.reshape(query_rows, width), codes], axis=1)
    spans = (lax.axis_size("z"), lax.axis_size("y"))
    combined = gather_bank(combined, spans).reshape(shards * query_rows, -1)
    offset_z = jnp.arange(spans[0], dtype=jnp.int32)
    sources = (lax.axis_index("z") - offset_z) % spans[0]
    group_queries = combined[:, :width].reshape(shards * query_rows, query_len, feature_dim)
    group_codes = combined[:, width : width + 2 * listed].astype(jnp.int32)

    owner_bank = group_codes[:, :listed].reshape(shards, entries)
    stored_at = group_codes[:, listed:].reshape(shards, entries)
    mine = owner_bank == me
    position = jnp.cumsum(mine.astype(jnp.int32), axis=1) - 1
    slot_ids = jnp.arange(capacity, dtype=jnp.int32)
    hit = mine[:, None, :] & (position[:, None, :] == slot_ids[None, :, None])
    entry_ids = jnp.arange(entries, dtype=jnp.int32)
    entry = jnp.sum(jnp.where(hit, entry_ids[None, None, :], 0), axis=2)
    local_slot = jnp.sum(jnp.where(hit, stored_at[:, None, :], 0), axis=2)
    picks = (entry // listed).reshape(-1)
    payload = holder_terms(
        local_slot.reshape(-1), picks, sources, group_queries, passages, shards, capacity, spans[1]
    )
    returned = lax.all_to_all(payload, BANK, 0, 0, tiled=True)

    holder = holder.reshape(entries)
    member = holder[:, None] == jnp.arange(shards, dtype=jnp.int32)[None, :]
    member = member.astype(jnp.int32)
    own_position = jnp.sum((jnp.cumsum(member, axis=0) - member) * member, axis=1)
    pieces = returned[:, capacity, 0, : capacity * 3].reshape(shards * capacity, 3)
    flat_slot = holder * capacity + own_position
    similarity = join3(pieces[flat_slot]).reshape(query_rows, listed)
    losses, coefficients = contrast(similarity, positive)
    slot_of = (holder * (capacity + 1) + own_position).reshape(query_rows, listed)
    rows = shards * (capacity + 1)
    spread = jnp.arange(rows, dtype=jnp.int32)[None, None, :] == slot_of[:, :, None]
    spread = jnp.sum(
        jnp.where(spread, coefficients[:, :, None].astype(jnp.float32), 0.0), axis=1
    ).astype(jnp.bfloat16)
    bases = returned.reshape(rows, query_len, feature_dim)
    gradient = jnp.einsum("qr,rid->qid", spread, bases, preferred_element_type=jnp.float32)
    return (losses, gradient)


def solution(mesh):
    rows = mesh.shape["query"]
    bank = mesh.shape["bank"]
    across = 4 if bank % 4 == 0 else 1
    devices = np.asarray(mesh.devices).reshape(rows, bank // across, across)
    split_mesh = Mesh(devices, ("query",) + BANK)
    every = ("query",) + BANK
    return jax.shard_map(
        body,
        mesh=split_mesh,
        in_specs=(
            P(every, None, None),
            P(BANK, None, None),
            P(),
            P(every, None),
            P(every),
        ),
        out_specs=(P(every), P(every, None, None)),
        check_vma=False,
    )
```

```python
import functools

import jax
import jax.numpy as jnp
import numpy as np
from jax import lax
from jax.experimental import pallas as pl
from jax.experimental.pallas import tpu as pltpu
from jax.sharding import Mesh
from jax.sharding import PartitionSpec as P

BANK = ("z", "y")


def contrast(similarity, positive):
    largest = jnp.max(similarity, axis=1, keepdims=True)
    raised = jnp.exp(similarity - largest)
    totals = jnp.sum(raised, axis=1, keepdims=True)
    picked = jnp.arange(similarity.shape[1], dtype=jnp.int32)[None, :] == positive[:, None]
    losses = (
        largest[:, 0] + jnp.log(totals[:, 0]) - jnp.sum(jnp.where(picked, similarity, 0.0), axis=1)
    )
    coefficients = (raised / totals - picked.astype(jnp.float32)).astype(jnp.bfloat16)
    return (losses, coefficients)


def join3(pieces):
    pieces = pieces.astype(jnp.float32)
    return (pieces[..., 0] + pieces[..., 1]) + pieces[..., 2]


def ring_gather(value, axis, size):
    def shift(x, step):
        return lax.ppermute(x, axis, [(i, (i + step) % size) for i in range(size)])

    right, left = [value], [value]
    for _ in range(size // 2):
        right.append(shift(right[-1], 1))
    for _ in range((size - 1) // 2):
        left.append(shift(left[-1], -1))
    return jnp.stack(right + left[1:][::-1], axis=0)


def gather_bank(value, shape):
    nearby = ring_gather(value, "y", shape[1])
    order = (lax.axis_index("y") - jnp.arange(shape[1], dtype=jnp.int32)) % shape[1]
    nearby = jnp.take(nearby, order, axis=0)
    return ring_gather(nearby, "z", shape[0])


def holder_kernel(capacity, group, per, slots_ref, picks_ref, sources_ref, queries_ref, *refs):
    tiles, (out_ref, scores_ref, weights_ref) = refs[: per * capacity], refs[per * capacity :]

    @pl.when(pl.program_id(0) == 0)
    def _():
        weights_ref[...] = jnp.zeros_like(weights_ref)

    for unit in range(per):
        source_terms(
            capacity, group, per, unit, picks_ref, queries_ref,
            tiles[unit * capacity : (unit + 1) * capacity], out_ref, scores_ref, weights_ref,
        )


def source_terms(capacity, group, per, unit, picks_ref, queries_ref, tiles, out_ref, scores_ref, weights_ref):
    source = pl.program_id(0) * per + unit
    query_rows = queries_ref.shape[0] // per
    query_len, feature_dim = queries_ref.shape[1], queries_ref.shape[2]
    tile_len = tiles[0].shape[1]
    stacked = jnp.concatenate([tiles[p][0] for p in range(capacity)], axis=0)
    block = queries_ref[unit * query_rows : (unit + 1) * query_rows].reshape(
        query_rows * query_len, feature_dim
    )
    scores_ref[...] = lax.dot_general(
        block, stacked, (((1,), (1,)), ((), ())), preferred_element_type=jnp.float32
    )
    lane = lax.broadcasted_iota(jnp.int32, (1, feature_dim), 1)
    row = jnp.zeros((1, feature_dim), jnp.float32)
    for p in range(capacity):
        pick = picks_ref[source * capacity + p]
        first = pl.multiple_of(pick * query_len, query_len)
        scores = scores_ref[pl.ds(first, query_len), pl.ds(p * tile_len, tile_len)]
        largest = jnp.max(scores, axis=1, keepdims=True)
        raised = jnp.exp(scores - largest)
        totals = jnp.sum(raised, axis=1, keepdims=True)
        maxima = largest + jnp.log(totals)
        g, r = p // group, p % group
        weights_ref[g, r * query_len : (r + 1) * query_len, r * tile_len : (r + 1) * tile_len] = (
            raised / totals
        ).astype(jnp.bfloat16)
        similarity = jnp.sum(maxima, axis=0, keepdims=True)
        high = similarity.astype(jnp.bfloat16).astype(jnp.float32)
        rest = similarity - high
        middle = rest.astype(jnp.bfloat16).astype(jnp.float32)
        low = rest - middle
        row = jnp.where(lane == 3 * p, high, row)
        row = jnp.where(lane == 3 * p + 1, middle, row)
        row = jnp.where(lane == 3 * p + 2, low, row)
    for g in range(capacity // group):
        basis = jnp.dot(
            weights_ref[g],
            stacked[g * group * tile_len : (g + 1) * group * tile_len],
            preferred_element_type=jnp.float32,
        )
        out_ref[unit, g * group : (g + 1) * group] = basis.astype(jnp.bfloat16).reshape(
            group, query_len, feature_dim
        )
    sublane = lax.broadcasted_iota(jnp.int32, (query_len, feature_dim), 0)
    out_ref[unit, capacity] = jnp.where(sublane == 0, row, 0.0).astype(jnp.bfloat16)


def holder_terms(slots, picks, sources, group_queries, passages, shards, capacity, per):
    query_rows = group_queries.shape[0] // shards
    steps = shards // per
    query_len, feature_dim = group_queries.shape[1], group_queries.shape[2]
    tile_len = passages.shape[1]

    def tile_spec(t):
        return pl.BlockSpec(
            (1, tile_len, feature_dim), lambda s, sl, pk, sr: (sl[s * per * capacity + t], 0, 0)
        )

    group = 1
    grid_spec = pltpu.PrefetchScalarGridSpec(
        num_scalar_prefetch=3,
        grid=(steps,),
        in_specs=[
            pl.BlockSpec((per * query_rows, query_len, feature_dim), lambda s, sl, pk, sr: (s, 0, 0))
        ]
        + [tile_spec(t) for t in range(per * capacity)],
        out_specs=pl.BlockSpec(
            (per, capacity + 1, query_len, feature_dim), lambda s, sl, pk, sr: (sr[s], 0, 0, 0)
        ),
        scratch_shapes=[
            pltpu.VMEM((query_rows * query_len, capacity * tile_len), jnp.float32),
            pltpu.VMEM((capacity // group, group * query_len, group * tile_len), jnp.bfloat16),
        ],
    )
    slots_total = shards * capacity
    flops = shards * 2 * feature_dim * capacity * tile_len * (query_rows * query_len + group * query_len)
    moved = slots_total * (tile_len + query_len) * feature_dim * 2
    return pl.pallas_call(
        functools.partial(holder_kernel, capacity, group, per),
        grid_spec=grid_spec,
        out_shape=jax.ShapeDtypeStruct(
            (shards, capacity + 1, query_len, feature_dim), jnp.bfloat16
        ),
        cost_estimate=pl.CostEstimate(
            flops=flops, transcendentals=slots_total * query_len * tile_len, bytes_accessed=moved
        ),
    )(slots, picks, sources, group_queries, *([passages] * (per * capacity)))


def body(queries, passages, passage_home, candidates, positive):
    shards = lax.axis_size(BANK)
    me = lax.axis_index(BANK)
    query_rows, query_len, feature_dim = queries.shape
    listed = candidates.shape[1]
    holdings = passages.shape[0]
    entries = query_rows * listed
    capacity = 3 * entries // shards
    width = query_len * feature_dim
    tail = 128

    own_storage = passage_home[candidates]
    holder = own_storage // holdings
    codes = jnp.concatenate(
        [holder, own_storage % holdings, jnp.zeros((query_rows, tail - 2 * listed), jnp.int32)],
        axis=1,
    ).astype(jnp.bfloat16)
    combined = jnp.concatenate([queries.reshape(query_rows, width), codes], axis=1)
    spans = (lax.axis_size("z"), lax.axis_size("y"))
    combined = gather_bank(combined, spans).reshape(shards * query_rows, -1)
    offset_z = jnp.arange(spans[0], dtype=jnp.int32)
    sources = (lax.axis_index("z") - offset_z) % spans[0]
    group_queries = combined[:, :width].reshape(shards * query_rows, query_len, feature_dim)
    group_codes = combined[:, width : width + 2 * listed].astype(jnp.int32)

    owner_bank = group_codes[:, :listed].reshape(shards, entries)
    stored_at = group_codes[:, listed:].reshape(shards, entries)
    mine = owner_bank == me
    position = jnp.cumsum(mine.astype(jnp.int32), axis=1) - 1
    slot_ids = jnp.arange(capacity, dtype=jnp.int32)
    hit = mine[:, None, :] & (position[:, None, :] == slot_ids[None, :, None])
    entry_ids = jnp.arange(entries, dtype=jnp.int32)
    entry = jnp.sum(jnp.where(hit, entry_ids[None, None, :], 0), axis=2)
    local_slot = jnp.sum(jnp.where(hit, stored_at[:, None, :], 0), axis=2)
    picks = (entry // listed).reshape(-1)
    payload = holder_terms(
        local_slot.reshape(-1), picks, sources, group_queries, passages, shards, capacity, spans[1]
    )
    returned = lax.all_to_all(payload, BANK, 0, 0, tiled=True)

    holder = holder.reshape(entries)
    member = holder[:, None] == jnp.arange(shards, dtype=jnp.int32)[None, :]
    member = member.astype(jnp.int32)
    own_position = jnp.sum((jnp.cumsum(member, axis=0) - member) * member, axis=1)
    pieces = returned[:, capacity, 0, : capacity * 3].reshape(shards * capacity, 3)
    flat_slot = holder * capacity + own_position
    similarity = join3(pieces[flat_slot]).reshape(query_rows, listed)
    losses, coefficients = contrast(similarity, positive)
    slot_of = (holder * (capacity + 1) + own_position).reshape(query_rows, listed)
    rows = shards * (capacity + 1)
    spread = jnp.arange(rows, dtype=jnp.int32)[None, None, :] == slot_of[:, :, None]
    spread = jnp.sum(
        jnp.where(spread, coefficients[:, :, None].astype(jnp.float32), 0.0), axis=1
    ).astype(jnp.bfloat16)
    bases = returned.reshape(rows, query_len, feature_dim)
    gradient = jnp.einsum("qr,rid->qid", spread, bases, preferred_element_type=jnp.float32)
    return (losses, gradient)


def solution(mesh):
    rows = mesh.shape["query"]
    bank = mesh.shape["bank"]
    across = 4 if bank % 4 == 0 else 1
    devices = np.asarray(mesh.devices).reshape(rows, bank // across, across)
    split_mesh = Mesh(devices, ("query",) + BANK)
    every = ("query",) + BANK
    return jax.shard_map(
        body,
        mesh=split_mesh,
        in_specs=(
            P(every, None, None),
            P(BANK, None, None),
            P(),
            P(every, None),
            P(every),
        ),
        out_specs=(P(every), P(every, None, None)),
        check_vma=False,
    )
```

```python
import functools

import jax
import jax.numpy as jnp
import numpy as np
from jax import lax
from jax.experimental import pallas as pl
from jax.experimental.pallas import tpu as pltpu
from jax.sharding import Mesh
from jax.sharding import PartitionSpec as P

BANK = ("z", "y")


def contrast(similarity, positive):
    largest = jnp.max(similarity, axis=1, keepdims=True)
    raised = jnp.exp(similarity - largest)
    totals = jnp.sum(raised, axis=1, keepdims=True)
    picked = jnp.arange(similarity.shape[1], dtype=jnp.int32)[None, :] == positive[:, None]
    losses = (
        largest[:, 0] + jnp.log(totals[:, 0]) - jnp.sum(jnp.where(picked, similarity, 0.0), axis=1)
    )
    coefficients = (raised / totals - picked.astype(jnp.float32)).astype(jnp.bfloat16)
    return (losses, coefficients)


def join3(pieces):
    pieces = pieces.astype(jnp.float32)
    return (pieces[..., 0] + pieces[..., 1]) + pieces[..., 2]


def ring_gather(value, axis, size):
    def shift(x, step):
        return lax.ppermute(x, axis, [(i, (i + step) % size) for i in range(size)])

    right, left = [value], [value]
    for _ in range(size // 2):
        right.append(shift(right[-1], 1))
    for _ in range((size - 1) // 2):
        left.append(shift(left[-1], -1))
    return jnp.stack(right + left[1:][::-1], axis=0)


def gather_bank(value, shape):
    nearby = ring_gather(value, "y", shape[1])
    order = (lax.axis_index("y") - jnp.arange(shape[1], dtype=jnp.int32)) % shape[1]
    nearby = jnp.take(nearby, order, axis=0)
    return ring_gather(nearby, "z", shape[0])


def holder_kernel(capacity, group, per, slots_ref, picks_ref, sources_ref, queries_ref, *refs):
    tiles, (out_ref, scores_ref, weights_ref) = refs[: per * capacity], refs[per * capacity :]

    @pl.when(pl.program_id(0) == 0)
    def _():
        weights_ref[...] = jnp.zeros_like(weights_ref)

    for unit in range(per):
        source_terms(
            capacity, group, per, unit, picks_ref, queries_ref,
            tiles[unit * capacity : (unit + 1) * capacity], out_ref, scores_ref, weights_ref,
        )


def source_terms(capacity, group, per, unit, picks_ref, queries_ref, tiles, out_ref, scores_ref, weights_ref):
    source = pl.program_id(0) * per + unit
    query_rows = queries_ref.shape[0] // per
    query_len, feature_dim = queries_ref.shape[1], queries_ref.shape[2]
    tile_len = tiles[0].shape[1]
    stacked = jnp.concatenate([tiles[p][0] for p in range(capacity)], axis=0)
    block = queries_ref[unit * query_rows : (unit + 1) * query_rows].reshape(
        query_rows * query_len, feature_dim
    )
    scores_ref[...] = lax.dot_general(
        block, stacked, (((1,), (1,)), ((), ())), preferred_element_type=jnp.float32
    )
    lane = lax.broadcasted_iota(jnp.int32, (1, feature_dim), 1)
    row = jnp.zeros((1, feature_dim), jnp.float32)
    for p in range(capacity):
        pick = picks_ref[source * capacity + p]
        first = pl.multiple_of(pick * query_len, query_len)
        scores = scores_ref[pl.ds(first, query_len), pl.ds(p * tile_len, tile_len)]
        largest = jnp.max(scores, axis=1, keepdims=True)
        raised = jnp.exp(scores - largest)
        totals = jnp.sum(raised, axis=1, keepdims=True)
        maxima = largest + jnp.log(totals)
        g, r = p // group, p % group
        weights_ref[g, r * query_len : (r + 1) * query_len, r * tile_len : (r + 1) * tile_len] = (
            raised / totals
        ).astype(jnp.bfloat16)
        similarity = jnp.sum(maxima, axis=0, keepdims=True)
        high = similarity.astype(jnp.bfloat16).astype(jnp.float32)
        rest = similarity - high
        middle = rest.astype(jnp.bfloat16).astype(jnp.float32)
        low = rest - middle
        row = jnp.where(lane == 3 * p, high, row)
        row = jnp.where(lane == 3 * p + 1, middle, row)
        row = jnp.where(lane == 3 * p + 2, low, row)
    for g in range(capacity // group):
        basis = jnp.dot(
            weights_ref[g],
            stacked[g * group * tile_len : (g + 1) * group * tile_len],
            preferred_element_type=jnp.float32,
        )
        out_ref[unit, g * group : (g + 1) * group] = basis.astype(jnp.bfloat16).reshape(
            group, query_len, feature_dim
        )
    sublane = lax.broadcasted_iota(jnp.int32, (query_len, feature_dim), 0)
    out_ref[unit, capacity] = jnp.where(sublane == 0, row, 0.0).astype(jnp.bfloat16)


def holder_terms(slots, picks, sources, group_queries, passages, shards, capacity, per):
    query_rows = group_queries.shape[0] // shards
    steps = shards // per
    query_len, feature_dim = group_queries.shape[1], group_queries.shape[2]
    tile_len = passages.shape[1]

    def tile_spec(t):
        return pl.BlockSpec(
            (1, tile_len, feature_dim), lambda s, sl, pk, sr: (sl[s * per * capacity + t], 0, 0)
        )

    group = 3 if capacity % 3 == 0 else 1
    grid_spec = pltpu.PrefetchScalarGridSpec(
        num_scalar_prefetch=3,
        grid=(steps,),
        in_specs=[
            pl.BlockSpec((per * query_rows, query_len, feature_dim), lambda s, sl, pk, sr: (s, 0, 0))
        ]
        + [tile_spec(t) for t in range(per * capacity)],
        out_specs=pl.BlockSpec(
            (per, capacity + 1, query_len, feature_dim), lambda s, sl, pk, sr: (sr[s], 0, 0, 0)
        ),
        scratch_shapes=[
            pltpu.VMEM((query_rows * query_len, capacity * tile_len), jnp.float32),
            pltpu.VMEM((capacity // group, group * query_len, group * tile_len), jnp.bfloat16),
        ],
    )
    slots_total = shards * capacity
    flops = shards * 2 * feature_dim * capacity * tile_len * (query_rows * query_len + group * query_len)
    moved = slots_total * (tile_len + query_len) * feature_dim * 2
    return pl.pallas_call(
        functools.partial(holder_kernel, capacity, group, per),
        grid_spec=grid_spec,
        out_shape=jax.ShapeDtypeStruct(
            (shards, capacity + 1, query_len, feature_dim), jnp.bfloat16
        ),
        cost_estimate=pl.CostEstimate(
            flops=flops, transcendentals=slots_total * query_len * tile_len, bytes_accessed=moved
        ),
    )(slots, picks, sources, group_queries, *([passages] * (per * capacity)))


def body(queries, passages, passage_home, candidates, positive):
    shards = lax.axis_size(BANK)
    me = lax.axis_index(BANK)
    query_rows, query_len, feature_dim = queries.shape
    listed = candidates.shape[1]
    holdings = passages.shape[0]
    entries = query_rows * listed
    capacity = 3 * entries // shards
    width = query_len * feature_dim
    tail = 128

    own_storage = passage_home[candidates]
    holder = own_storage // holdings
    codes = jnp.concatenate(
        [holder, own_storage % holdings, jnp.zeros((query_rows, tail - 2 * listed), jnp.int32)],
        axis=1,
    ).astype(jnp.bfloat16)
    combined = jnp.concatenate([queries.reshape(query_rows, width), codes], axis=1)
    spans = (lax.axis_size("z"), lax.axis_size("y"))
    combined = gather_bank(combined, spans).reshape(shards * query_rows, -1)
    offset_z = jnp.arange(spans[0], dtype=jnp.int32)
    sources = (lax.axis_index("z") - offset_z) % spans[0]
    group_queries = combined[:, :width].reshape(shards * query_rows, query_len, feature_dim)
    group_codes = combined[:, width : width + 2 * listed].astype(jnp.int32)

    owner_bank = group_codes[:, :listed].reshape(shards, entries)
    stored_at = group_codes[:, listed:].reshape(shards, entries)
    mine = owner_bank == me
    position = jnp.cumsum(mine.astype(jnp.int32), axis=1) - 1
    slot_ids = jnp.arange(capacity, dtype=jnp.int32)
    hit = mine[:, None, :] & (position[:, None, :] == slot_ids[None, :, None])
    entry_ids = jnp.arange(entries, dtype=jnp.int32)
    entry = jnp.sum(jnp.where(hit, entry_ids[None, None, :], 0), axis=2)
    local_slot = jnp.sum(jnp.where(hit, stored_at[:, None, :], 0), axis=2)
    picks = (entry // listed).reshape(-1)
    payload = holder_terms(
        local_slot.reshape(-1), picks, sources, group_queries, passages, shards, capacity, spans[1]
    )
    returned = lax.all_to_all(payload, BANK, 0, 0, tiled=True)

    holder = holder.reshape(entries)
    member = holder[:, None] == jnp.arange(shards, dtype=jnp.int32)[None, :]
    member = member.astype(jnp.int32)
    own_position = jnp.sum((jnp.cumsum(member, axis=0) - member) * member, axis=1)
    pieces = returned[:, capacity, 0, : capacity * 3].reshape(shards * capacity, 3)
    flat_slot = holder * capacity + own_position
    similarity = join3(pieces[flat_slot]).reshape(query_rows, listed)
    losses, coefficients = contrast(similarity, positive)
    slot_of = (holder * (capacity + 1) + own_position).reshape(query_rows, listed)
    rows = shards * (capacity + 1)
    spread = jnp.arange(rows, dtype=jnp.int32)[None, None, :] == slot_of[:, :, None]
    spread = jnp.sum(
        jnp.where(spread, coefficients[:, :, None].astype(jnp.float32), 0.0), axis=1
    ).astype(jnp.bfloat16)
    bases = returned.reshape(rows, query_len, feature_dim)
    gradient = jnp.einsum("qr,rid->qid", spread, bases, preferred_element_type=jnp.float32)
    return (losses, gradient)


def solution(mesh):
    rows = mesh.shape["query"]
    bank = mesh.shape["bank"]
    across = 4 if bank % 4 == 0 else 1
    devices = np.asarray(mesh.devices).reshape(rows, bank // across, across)
    split_mesh = Mesh(devices, ("query",) + BANK)
    every = ("query",) + BANK
    return jax.shard_map(
        body,
        mesh=split_mesh,
        in_specs=(
            P(every, None, None),
            P(BANK, None, None),
            P(),
            P(every, None),
            P(every),
        ),
        out_specs=(P(every), P(every, None, None)),
        check_vma=False,
    )
```
